512 devices in a mesh: bx: 32 (over x, z_hi, core), by: 16 (over y, z_lo).
Axes of the slice: x: 4, y: 8, z: 8 (z_hi: 4, z_lo: 2; z = z_hi * 2 + z_lo), core: 2. Of those that a mesh axis runs over, the one named last changes fastest.
Arguments:
- adjoint_start: float32 [6, 512, 256, 128], P(None, 'bx', 'by'), may hold values from -6 to 6
- objective_grad: float32 [6, 512, 256, 128], P(None, 'bx', 'by'), may hold values from -4 to 4
- spectral_radius: float32 [3, 512, 256, 128], P(None, 'bx', 'by'), may hold values from 0.5 to 4
- local_step: float32 [512, 256, 128], P('bx', 'by'), may hold values from 0.02 to 0.12
- flux_jacobian: float32 [3, 6, 6], replicated, may hold values from -2.5 to 2.5
- face_orient: int32 [32, 2], P('bx'), may hold values from 0 to 1, as said below
- wall_count: int32 [32, 16], P('bx', 'by'), may hold values from 0 to 256
- face_patch: int32 [512, 256], P('bx', 'by'), may hold values from 0 to 2047
- face_area: float32 [512, 256], P('bx', 'by'), may hold values from 1 to 10
- force_weight: float32 [6], replicated, may hold values from -3 to 3
Outputs:
- adjoint_next: float32 [6, 512, 256, 128], P(None, 'bx', 'by')
- patch_force: float32 [2048], P(('bx', 'by'))
The draws below stay inside these ranges and needn't reach their ends.
Inputs may be any that keep to these rules, and one draw needn't show every extreme that they name: face_orient[a, 1] equals face_orient[a + 1, 0]; a 1 marks a face between block rows whose matched cells run in reverse order along the third direction.
All inputs are finite; a program needn't handle non-finite values.
Results may differ from the reference program's by a relative error of at most 0.00012.
Values sent between devices are 32-bit elements; how exact they have to be, the bound alone decides.
No kernel may reach another device: no remote copies, remote signals or barrier semaphores. Data moves between devices by JAX's collectives and lax.ppermute only.
A program may use at most 64 MiB of HBM per device.

```python
import math
import jax
import jax.numpy as jnp
from jax import lax

FIELDS = 6
CI = 16
CJ = 16
CK = 128
NX = 512
NY = 256
PATCHES = 2048
N_BX = 32
N_BY = 16


def draw_face_orient(key, part):
    flags = jax.random.randint(key, (N_BX + 1,), 0, 2)
    return jnp.stack([flags[:-1], flags[1:]], axis=1).astype(jnp.int32)


def with_ends(drawn, own_key, low, largest):
    longest = drawn.shape.index(max(drawn.shape))
    spots = []
    for shift in (0, 1):
        where = [jax.random.randint(jax.random.fold_in(own_key, axis), (), 0, length) for axis, length in enumerate(drawn.shape)]
        where[longest] = (where[longest] + shift) % drawn.shape[longest]
        spots.append(tuple(where))
    return drawn.at[spots[0]].set(low).at[spots[1]].set(largest)


def levels(rng, extent, cuts, low, top_value):
    gain, own = 1.0, jax.random.fold_in(rng, 6)
    for axis_at, parts in cuts:
        steps = jnp.exp(jax.random.uniform(jax.random.fold_in(own, axis_at), (parts,), jnp.float32, low / len(cuts), top_value / len(cuts)))
        gain = gain * jnp.repeat(steps, extent[axis_at] // parts).reshape([-1 if axis == axis_at else 1 for axis in range(len(extent))])
    return gain


def normal_values(rng, dims, scale, limit, shards=(), dtype=jnp.bfloat16):
    drawn = jax.random.normal(rng, dims, jnp.float32) * scale
    if len(shards) > 0:
        drawn = levels(rng, dims, shards, -0.22, 0.18) * drawn
    return jnp.clip(drawn, min=-limit, max=limit).astype(dtype)


def setup_inputs(seed: int = 0) -> dict:
    seeds = jax.random.split(jax.random.key(seed), 11)
    return {
        "adjoint_start": normal_values(seeds[0], (FIELDS, NX, NY, CK), 1.0, 6.0, ((1, 32), (2, 16)), jnp.float32),
        "objective_grad": normal_values(seeds[1], (FIELDS, NX, NY, CK), 0.5, 4.0, ((1, 32), (2, 16)), jnp.float32),
        "spectral_radius": jnp.clip(jnp.exp(math.log(4.0) - 2.0794415 * jax.random.uniform(seeds[2], (3, NX, NY, CK), jnp.float32) ** levels(seeds[2], (3, NX, NY, CK), ((1, 32), (2, 16)), -0.2, 0.2)), 0.5, 4.0),
        "local_step": jnp.clip(jnp.exp(math.log(0.12) - 1.7917595 * jax.random.uniform(seeds[3], (NX, NY, CK), jnp.float32) ** levels(seeds[3], (NX, NY, CK), ((0, 32), (1, 16)), -0.2, 0.2)), 0.02, 0.12),
        "flux_jacobian": normal_values(seeds[4], (3, FIELDS, FIELDS), FIELDS ** -0.5, 2.5, (), jnp.float32),
        "face_orient": draw_face_orient(jax.random.fold_in(seeds[10], 71), 0),
        "wall_count": with_ends(jax.random.randint(seeds[6], (N_BX, N_BY), 0, CI * CJ + 1), jax.random.fold_in(seeds[6], 1), 0, CI * CJ).astype(jnp.int32),
        "face_patch": with_ends(jax.random.randint(seeds[7], (NX, NY), 0, PATCHES), jax.random.fold_in(seeds[7], 1), 0, PATCHES - 1).astype(jnp.int32),
        "face_area": jnp.clip(jnp.exp(math.log(10.0) - 2.3025851 * jax.random.uniform(seeds[8], (NX, NY), jnp.float32) ** levels(seeds[8], (NX, NY), ((0, 32), (1, 16)), -0.2, 0.2)), 1.0, 10.0),
        "force_weight": normal_values(seeds[9], (FIELDS,), 1.0, 3.0, (), jnp.float32),
    }


EPS = 0.1


def shift_zero(field, offset, axis):
    count = field.shape[axis]
    widths = [(0, 0)] * field.ndim
    widths[axis] = (2, 2)
    padded = jnp.pad(field, widths)
    return lax.slice_in_dim(padded, 2 + offset, 2 + offset + count, axis=axis)


def across_rows(field, offset, face_orient):
    shifted = shift_zero(field, offset, 1)
    rowpos = jnp.arange(NX) % CI
    block_row = jnp.arange(NX) // CI
    if offset < 0:
        cross = rowpos < -offset
        flagged = face_orient[block_row, 0] == 1
    else:
        cross = rowpos >= CI - offset
        flagged = face_orient[block_row, 1] == 1
    use = (cross & flagged)[None, :, None, None]
    return jnp.where(use, jnp.flip(shifted, 3), shifted)


def transpose_apply(matrix, field):
    return jnp.einsum('fg,fxyz->gxyz', matrix, field, precision=lax.Precision.HIGHEST)


def operate(field, radius, flux_jacobian, face_orient):
    summed = jnp.zeros_like(field)
    for direction in range(3):
        if direction == 0:
            front_one = across_rows(field, 1, face_orient)
            back_one = across_rows(field, -1, face_orient)
            front_two = across_rows(field, 2, face_orient)
            back_two = across_rows(field, -2, face_orient)
        else:
            front_one = shift_zero(field, 1, direction + 1)
            back_one = shift_zero(field, -1, direction + 1)
            front_two = shift_zero(field, 2, direction + 1)
            back_two = shift_zero(field, -2, direction + 1)
        if direction == 2:
            coupled = transpose_apply(flux_jacobian[direction], front_one + back_one)
        else:
            coupled = transpose_apply(flux_jacobian[direction], front_one - back_one)
        fourth = front_two - 4.0 * front_one + 6.0 * field - 4.0 * back_one + back_two
        summed = summed + radius[direction] * (0.5 * coupled + EPS * fourth)
    return summed


def reference(adjoint_start, objective_grad, spectral_radius, local_step, flux_jacobian, face_orient, wall_count, face_patch, face_area, force_weight):
    counts_full = jnp.repeat(jnp.repeat(wall_count, CI, axis=0), CJ, axis=1)
    position = (jnp.arange(NX) % CI)[:, None] * CJ + (jnp.arange(NY) % CJ)[None, :]
    live = (position < counts_full).astype(jnp.float32)
    wall_adjoint = jnp.einsum('f,fxy->xy', force_weight, adjoint_start[:, :, :, 0], precision=lax.Precision.HIGHEST)
    weighted_area = live * face_area
    wall_value = weighted_area * wall_adjoint
    patch_ids = face_patch.reshape(-1).astype(jnp.int32)
    patch_sum = jax.ops.segment_sum(wall_value.reshape(-1), patch_ids, num_segments=PATCHES)
    patch_area = jax.ops.segment_sum(weighted_area.reshape(-1), patch_ids, num_segments=PATCHES)
    patch_force = patch_sum / (1.0 + patch_area)
    face_force = weighted_area * patch_force[face_patch]
    source = objective_grad.at[:, :, :, 0].add(force_weight[:, None, None] * face_force[None])
    section_one = adjoint_start - 0.5 * local_step * (operate(adjoint_start, spectral_radius, flux_jacobian, face_orient) + source)
    adjoint_next = adjoint_start - local_step * (operate(section_one, spectral_radius, flux_jacobian, face_orient) + source)
    return adjoint_next, patch_force
```

```python
import jax
import jax.numpy as jnp
from jax import lax
from jax.sharding import PartitionSpec as P

P_DEV = 4
REDUCE_LEN = 16384

EPS = 0.1


def neighbour_rims(shard, axis, dim, width):
    devices, length = lax.axis_size(axis), shard.shape[dim]
    up = [(i, i + 1) for i in range(devices - 1)]
    down = [(j, i) for i, j in up]
    last = lax.slice_in_dim(shard, length - width, length, axis=dim)
    first = lax.slice_in_dim(shard, 0, width, axis=dim)
    before = lax.ppermute(last, axis, up)
    after = lax.ppermute(first, axis, down)
    return before, after


def halos(field, low_flag, high_flag):
    lo_i, hi_i = neighbour_rims(field, "bx", 1, 2)
    lo_j, hi_j = neighbour_rims(field, "by", 2, 2)
    lo_i = jnp.where(low_flag == 1, jnp.flip(lo_i, 3), lo_i)
    hi_i = jnp.where(high_flag == 1, jnp.flip(hi_i, 3), hi_i)
    return lo_i, hi_i, lo_j, hi_j


def operate(center, rims, radius, flux_jacobian):
    lo_i, hi_i, lo_j, hi_j = rims
    rows_i, rows_j, depth = center.shape[1:]
    ext_i = jnp.concatenate([lo_i, center, hi_i], axis=1)
    ext_j = jnp.concatenate([lo_j, center, hi_j], axis=2)
    padded_k = jnp.pad(center, ((0, 0), (0, 0), (0, 0), (2, 2)))

    def along_first(offset):
        return ext_i[:, 2 + offset : 2 + offset + rows_i]

    def along_second(offset):
        return ext_j[:, :, 2 + offset : 2 + offset + rows_j]

    def along_third(offset):
        return padded_k[:, :, :, 2 + offset : 2 + offset + depth]

    summed = None
    for direction, slicer in ((0, along_first), (1, along_second), (2, along_third)):
        front_one = slicer(1)
        back_one = slicer(-1)
        fourth = slicer(2) - 4.0 * front_one + 6.0 * center - 4.0 * back_one + slicer(-2)
        diff = front_one + back_one if direction == 2 else front_one - back_one
        jac = flux_jacobian[direction]
        coupled = jnp.stack(
            [sum(jac[f, g] * diff[f] for f in range(diff.shape[0])) for g in range(diff.shape[0])]
        )
        term = radius[direction] * (0.5 * coupled + EPS * fourth)
        summed = term if summed is None else summed + term
    return summed


def plane_stencil(own, lo, hi, axis):
    ext = jnp.concatenate([lo, own, hi], axis=axis)
    n = own.shape[axis]

    def at(offset):
        return lax.slice_in_dim(ext, 2 + offset, 2 + offset + n, axis=axis)

    first = at(1) - at(-1)
    fourth = at(2) - 4.0 * at(1) + 6.0 * own - 4.0 * at(-1) + at(-2)
    return first, fourth


def local(
    adjoint_start,
    objective_grad,
    spectral_radius,
    local_step,
    flux_jacobian,
    face_orient,
    wall_count,
    face_patch,
    face_area,
    force_weight,
):
    fields, rows_i, rows_j, depth = adjoint_start.shape
    patch_total = P_DEV * lax.axis_size("bx") * lax.axis_size("by")
    low_flag = face_orient[0, 0]
    high_flag = face_orient[0, 1]
    position = jnp.arange(rows_i)[:, None] * rows_j + jnp.arange(rows_j)[None, :]
    live = (position < wall_count[0, 0]).astype(jnp.float32)
    weighted_area = live * face_area
    wall_adjoint = jnp.einsum(
        "f,fxy->xy", force_weight, adjoint_start[:, :, :, 0], precision=lax.Precision.HIGHEST
    )
    wall_value = (weighted_area * wall_adjoint).reshape(-1)
    patch_ids = face_patch.reshape(-1)
    table = (patch_ids[:, None] == jnp.arange(patch_total)[None, :]).astype(jnp.float32)
    local_sum = jnp.dot(wall_value, table, precision=lax.Precision.HIGHEST)
    local_area = jnp.dot(weighted_area.reshape(-1), table, precision=lax.Precision.HIGHEST)
    padding = jnp.zeros((max(REDUCE_LEN - 2 * patch_total, 0),), jnp.float32)
    with jax.named_scope("reduce"):
        summed = lax.psum(jnp.concatenate([local_sum, local_area, padding]), ("bx", "by"))

    step_area = local_step[:, :, 0] * weighted_area
    column = jnp.stack([step_area, face_patch.astype(jnp.float32)])
    col_lo_i, col_hi_i = neighbour_rims(column, "bx", 1, 2)
    col_lo_j, col_hi_j = neighbour_rims(column, "by", 2, 2)

    radius = spectral_radius
    with jax.named_scope("first"):
        rims = halos(adjoint_start, low_flag, high_flag)
        section_part = adjoint_start - 0.5 * local_step * (
            operate(adjoint_start, rims, radius, flux_jacobian) + objective_grad
        )
    with jax.named_scope("second"):
        rims = halos(section_part, low_flag, high_flag)
        next_part = adjoint_start - local_step * (
            operate(section_part, rims, radius, flux_jacobian) + objective_grad
        )
    summed, next_part = lax.optimization_barrier((summed, next_part))

    every_force = summed[:patch_total] / (1.0 + summed[patch_total : 2 * patch_total])
    start_own = lax.axis_index(("bx", "by")) * P_DEV
    patch_force = lax.dynamic_slice_in_dim(every_force, start_own, P_DEV, 0)

    def force_of(ids):
        flat = ids.reshape(-1, 1).astype(jnp.int32)
        hit = (flat == jnp.arange(patch_total)[None, :]).astype(jnp.float32)
        return jnp.dot(hit, every_force, precision=lax.Precision.HIGHEST).reshape(ids.shape)

    face_force = weighted_area * force_of(face_patch.reshape(-1)).reshape(rows_i, rows_j)
    g_own = local_step[:, :, 0] * face_force
    g_lo_i = col_lo_i[0] * force_of(col_lo_i[1])
    g_hi_i = col_hi_i[0] * force_of(col_hi_i[1])
    g_lo_j = col_lo_j[0] * force_of(col_lo_j[1])
    g_hi_j = col_hi_j[0] * force_of(col_hi_j[1])
    zero_i = jnp.zeros_like(g_lo_i)
    first_i0, fourth_i0 = plane_stencil(
        g_own,
        jnp.where(low_flag == 1, zero_i, g_lo_i),
        jnp.where(high_flag == 1, zero_i, g_hi_i),
        0,
    )
    first_ik, fourth_ik = plane_stencil(
        jnp.zeros_like(g_own),
        jnp.where(low_flag == 1, g_lo_i, zero_i),
        jnp.where(high_flag == 1, g_hi_i, zero_i),
        0,
    )
    first_j, fourth_j = plane_stencil(g_own, g_lo_j, g_hi_j, 1)

    kk = jnp.arange(depth)[None, None, :]
    at0 = kk == 0
    atk = kk == depth - 1
    first_i = jnp.where(at0, first_i0[:, :, None], jnp.where(atk, first_ik[:, :, None], 0.0))
    fourth_i = jnp.where(at0, fourth_i0[:, :, None], jnp.where(atk, fourth_ik[:, :, None], 0.0))
    first_j3 = jnp.where(at0, first_j[:, :, None], 0.0)
    fourth_j3 = jnp.where(at0, fourth_j[:, :, None], 0.0)
    g3 = g_own[:, :, None]
    sum_k = jnp.where(kk == 1, g3, 0.0)
    fourth_k = jnp.where(at0, 6.0 * g3, jnp.where(kk == 1, -4.0 * g3, jnp.where(kk == 2, g3, 0.0)))
    wall3 = jnp.where(at0, face_force[:, :, None], 0.0)

    coupled_w = [
        jnp.sum(flux_jacobian[d] * force_weight[:, None], axis=0) for d in range(3)
    ]
    correction = []
    for g in range(fields):
        spread = (
            radius[0] * (0.5 * coupled_w[0][g] * first_i + EPS * force_weight[g] * fourth_i)
            + radius[1] * (0.5 * coupled_w[1][g] * first_j3 + EPS * force_weight[g] * fourth_j3)
            + radius[2] * (0.5 * coupled_w[2][g] * sum_k + EPS * force_weight[g] * fourth_k)
        )
        correction.append(force_weight[g] * wall3 - 0.5 * spread)
    adjoint_next = next_part - local_step * jnp.stack(correction)
    return (adjoint_next, patch_force)


def solution(mesh):
    in_specs = (
        P(None, "bx", "by", None),
        P(None, "bx", "by", None),
        P(None, "bx", "by", None),
        P("bx", "by", None),
        P(),
        P("bx", None),
        P("bx", "by"),
        P("bx", "by"),
        P("bx", "by"),
        P(),
    )
    out_specs = (P(None, "bx", "by", None), P(("bx", "by")))
    return jax.shard_map(local, mesh=mesh, in_specs=in_specs, out_specs=out_specs, check_vma=False)
```

```python
import jax
import jax.numpy as jnp
from jax import lax
from jax.sharding import PartitionSpec as P

P_DEV = 4

EPS = 0.1


def neighbour_rims(shard, axis, dim, width):
    devices, length = lax.axis_size(axis), shard.shape[dim]
    up = [(i, i + 1) for i in range(devices - 1)]
    down = [(j, i) for i, j in up]
    last = lax.slice_in_dim(shard, length - width, length, axis=dim)
    first = lax.slice_in_dim(shard, 0, width, axis=dim)
    before = lax.ppermute(last, axis, up)
    after = lax.ppermute(first, axis, down)
    return before, after


def butterfly_sum(x, axes):
    for axis in axes:
        devices = lax.axis_size(axis)
        bit = 1
        while bit < devices:
            pairs = [(i, i ^ bit) for i in range(devices)]
            x = x + lax.ppermute(x, axis, pairs)
            bit *= 2
    return x


def halos(field, low_flag, high_flag):
    lo_i, hi_i = neighbour_rims(field, "bx", 1, 2)
    lo_j, hi_j = neighbour_rims(field, "by", 2, 2)
    lo_i = jnp.where(low_flag == 1, jnp.flip(lo_i, 3), lo_i)
    hi_i = jnp.where(high_flag == 1, jnp.flip(hi_i, 3), hi_i)
    return lo_i, hi_i, lo_j, hi_j


def operate(center, rims, radius, flux_jacobian):
    lo_i, hi_i, lo_j, hi_j = rims
    rows_i, rows_j, depth = center.shape[1:]
    ext_i = jnp.concatenate([lo_i, center, hi_i], axis=1)
    ext_j = jnp.concatenate([lo_j, center, hi_j], axis=2)
    padded_k = jnp.pad(center, ((0, 0), (0, 0), (0, 0), (2, 2)))

    def along_first(offset):
        return ext_i[:, 2 + offset : 2 + offset + rows_i]

    def along_second(offset):
        return ext_j[:, :, 2 + offset : 2 + offset + rows_j]

    def along_third(offset):
        return padded_k[:, :, :, 2 + offset : 2 + offset + depth]

    summed = None
    for direction, slicer in ((0, along_first), (1, along_second), (2, along_third)):
        front_one = slicer(1)
        back_one = slicer(-1)
        fourth = slicer(2) - 4.0 * front_one + 6.0 * center - 4.0 * back_one + slicer(-2)
        diff = front_one + back_one if direction == 2 else front_one - back_one
        coupled = jnp.einsum(
            "fg,fxyz->gxyz", flux_jacobian[direction], diff, precision=lax.Precision.HIGHEST
        )
        term = radius[direction] * (0.5 * coupled + EPS * fourth)
        summed = term if summed is None else summed + term
    return summed


def plane_stencil(own, lo, hi, axis):
    ext = jnp.concatenate([lo, own, hi], axis=axis)
    n = own.shape[axis]

    def at(offset):
        return lax.slice_in_dim(ext, 2 + offset, 2 + offset + n, axis=axis)

    first = at(1) - at(-1)
    fourth = at(2) - 4.0 * at(1) + 6.0 * own - 4.0 * at(-1) + at(-2)
    return first, fourth


def local(
    adjoint_start,
    objective_grad,
    spectral_radius,
    local_step,
    flux_jacobian,
    face_orient,
    wall_count,
    face_patch,
    face_area,
    force_weight,
):
    fields, rows_i, rows_j, depth = adjoint_start.shape
    patch_total = P_DEV * lax.axis_size("bx") * lax.axis_size("by")
    low_flag = face_orient[0, 0]
    high_flag = face_orient[0, 1]
    position = jnp.arange(rows_i)[:, None] * rows_j + jnp.arange(rows_j)[None, :]
    live = (position < wall_count[0, 0]).astype(jnp.float32)
    weighted_area = live * face_area
    wall_adjoint = jnp.einsum(
        "f,fxy->xy", force_weight, adjoint_start[:, :, :, 0], precision=lax.Precision.HIGHEST
    )
    wall_value = (weighted_area * wall_adjoint).reshape(-1)
    patch_ids = face_patch.reshape(-1)
    table = (patch_ids[:, None] == jnp.arange(patch_total)[None, :]).astype(jnp.float32)
    local_sum = jnp.dot(wall_value, table, precision=lax.Precision.HIGHEST)
    local_area = jnp.dot(weighted_area.reshape(-1), table, precision=lax.Precision.HIGHEST)
    summed = butterfly_sum(jnp.concatenate([local_sum, local_area]), ("bx", "by"))

    step_area = local_step[:, :, 0] * weighted_area
    column = jnp.stack([step_area, face_patch.astype(jnp.float32)])
    col_lo_i, col_hi_i = neighbour_rims(column, "bx", 1, 2)
    col_lo_j, col_hi_j = neighbour_rims(column, "by", 2, 2)

    radius = spectral_radius
    with jax.named_scope("first"):
        rims = halos(adjoint_start, low_flag, high_flag)
        section_part = adjoint_start - 0.5 * local_step * (
            operate(adjoint_start, rims, radius, flux_jacobian) + objective_grad
        )
    with jax.named_scope("second"):
        rims = halos(section_part, low_flag, high_flag)
        next_part = adjoint_start - local_step * (
            operate(section_part, rims, radius, flux_jacobian) + objective_grad
        )
    summed, next_part = lax.optimization_barrier((summed, next_part))

    every_force = summed[:patch_total] / (1.0 + summed[patch_total : 2 * patch_total])
    start_own = lax.axis_index(("bx", "by")) * P_DEV
    patch_force = lax.dynamic_slice_in_dim(every_force, start_own, P_DEV, 0)

    def force_of(ids):
        flat = ids.reshape(-1, 1).astype(jnp.int32)
        hit = (flat == jnp.arange(patch_total)[None, :]).astype(jnp.float32)
        return jnp.dot(hit, every_force, precision=lax.Precision.HIGHEST).reshape(ids.shape)

    ids = jnp.concatenate(
        [face_patch.reshape(-1).astype(jnp.float32)]
        + [rim[1].reshape(-1) for rim in (col_lo_i, col_hi_i, col_lo_j, col_hi_j)]
    )
    forces = force_of(ids)
    cut = rows_i * rows_j
    face_force = weighted_area * forces[:cut].reshape(rows_i, rows_j)
    g_own = local_step[:, :, 0] * face_force
    rim_forces = []
    for rim in (col_lo_i, col_hi_i, col_lo_j, col_hi_j):
        size = rim[1].size
        rim_forces.append(rim[0] * forces[cut : cut + size].reshape(rim[1].shape))
        cut += size
    g_lo_i, g_hi_i, g_lo_j, g_hi_j = rim_forces
    zero_i = jnp.zeros_like(g_lo_i)
    first_i0, fourth_i0 = plane_stencil(
        g_own,
        jnp.where(low_flag == 1, zero_i, g_lo_i),
        jnp.where(high_flag == 1, zero_i, g_hi_i),
        0,
    )
    first_ik, fourth_ik = plane_stencil(
        jnp.zeros_like(g_own),
        jnp.where(low_flag == 1, g_lo_i, zero_i),
        jnp.where(high_flag == 1, g_hi_i, zero_i),
        0,
    )
    first_j, fourth_j = plane_stencil(g_own, g_lo_j, g_hi_j, 1)

    kk = jnp.arange(depth)[None, None, :]
    at0 = kk == 0
    atk = kk == depth - 1
    first_i = jnp.where(at0, first_i0[:, :, None], jnp.where(atk, first_ik[:, :, None], 0.0))
    fourth_i = jnp.where(at0, fourth_i0[:, :, None], jnp.where(atk, fourth_ik[:, :, None], 0.0))
    first_j3 = jnp.where(at0, first_j[:, :, None], 0.0)
    fourth_j3 = jnp.where(at0, fourth_j[:, :, None], 0.0)
    g3 = g_own[:, :, None]
    sum_k = jnp.where(kk == 1, g3, 0.0)
    fourth_k = jnp.where(at0, 6.0 * g3, jnp.where(kk == 1, -4.0 * g3, jnp.where(kk == 2, g3, 0.0)))
    wall3 = jnp.where(at0, face_force[:, :, None], 0.0)

    coupled_w = jnp.einsum(
        "dfg,f->dg", flux_jacobian, force_weight, precision=lax.Precision.HIGHEST
    )[:, :, None, None, None]
    weight = force_weight[:, None, None, None]
    spread = (
        radius[0] * (0.5 * coupled_w[0] * first_i + EPS * weight * fourth_i)
        + radius[1] * (0.5 * coupled_w[1] * first_j3 + EPS * weight * fourth_j3)
        + radius[2] * (0.5 * coupled_w[2] * sum_k + EPS * weight * fourth_k)
    )
    correction = weight * wall3 - 0.5 * spread
    adjoint_next = next_part - local_step * correction
    return (adjoint_next, patch_force)


def solution(mesh):
    in_specs = (
        P(None, "bx", "by", None),
        P(None, "bx", "by", None),
        P(None, "bx", "by", None),
        P("bx", "by", None),
        P(),
        P("bx", None),
        P("bx", "by"),
        P("bx", "by"),
        P("bx", "by"),
        P(),
    )
    out_specs = (P(None, "bx", "by", None), P(("bx", "by")))
    return jax.shard_map(local, mesh=mesh, in_specs=in_specs, out_specs=out_specs, check_vma=False)
```

```python
import jax
import jax.numpy as jnp
from jax import lax
from jax.sharding import PartitionSpec as P

P_DEV = 4

EPS = 0.1


def neighbour_rims(shard, axis, dim, width):
    devices, length = lax.axis_size(axis), shard.shape[dim]
    up = [(i, i + 1) for i in range(devices - 1)]
    down = [(j, i) for i, j in up]
    last = lax.slice_in_dim(shard, length - width, length, axis=dim)
    first = lax.slice_in_dim(shard, 0, width, axis=dim)
    before = lax.ppermute(last, axis, up)
    after = lax.ppermute(first, axis, down)
    return before, after


def butterfly_sum(x, axes):
    for axis in axes:
        devices = lax.axis_size(axis)
        bit = 1
        while bit < devices:
            pairs = [(i, i ^ bit) for i in range(devices)]
            x = x + lax.ppermute(x, axis, pairs)
            bit *= 2
    return x


def halos(field, low_flag, high_flag, extra=None):
    if extra is not None:
        field = jnp.concatenate([field, extra], axis=0)
    lo_i, hi_i = neighbour_rims(field, "bx", 1, 2)
    lo_j, hi_j = neighbour_rims(field, "by", 2, 2)
    extras = None
    if extra is not None:
        count = extra.shape[0]
        extras = tuple(rim[-count:] for rim in (lo_i, hi_i, lo_j, hi_j))
        lo_i, hi_i, lo_j, hi_j = (rim[:-count] for rim in (lo_i, hi_i, lo_j, hi_j))
    lo_i = jnp.where(low_flag == 1, jnp.flip(lo_i, 3), lo_i)
    hi_i = jnp.where(high_flag == 1, jnp.flip(hi_i, 3), hi_i)
    return (lo_i, hi_i, lo_j, hi_j), extras


def operate(center, rims, radius, flux_jacobian):
    lo_i, hi_i, lo_j, hi_j = rims
    rows_i, rows_j, depth = center.shape[1:]
    ext_i = jnp.concatenate([lo_i, center, hi_i], axis=1)
    ext_j = jnp.concatenate([lo_j, center, hi_j], axis=2)
    padded_k = jnp.pad(center, ((0, 0), (0, 0), (0, 0), (2, 2)))

    def along_first(offset):
        return ext_i[:, 2 + offset : 2 + offset + rows_i]

    def along_second(offset):
        return ext_j[:, :, 2 + offset : 2 + offset + rows_j]

    def along_third(offset):
        return padded_k[:, :, :, 2 + offset : 2 + offset + depth]

    summed = None
    for direction, slicer in ((0, along_first), (1, along_second), (2, along_third)):
        front_one = slicer(1)
        back_one = slicer(-1)
        fourth = slicer(2) - 4.0 * front_one + 6.0 * center - 4.0 * back_one + slicer(-2)
        diff = front_one + back_one if direction == 2 else front_one - back_one
        coupled = jnp.einsum(
            "fg,fxyz->gxyz", flux_jacobian[direction], diff, precision=lax.Precision.HIGHEST
        )
        term = radius[direction] * (0.5 * coupled + EPS * fourth)
        summed = term if summed is None else summed + term
    return summed


def plane_stencil(own, lo, hi, axis):
    ext = jnp.concatenate([lo, own, hi], axis=axis)
    n = own.shape[axis]

    def at(offset):
        return lax.slice_in_dim(ext, 2 + offset, 2 + offset + n, axis=axis)

    first = at(1) - at(-1)
    fourth = at(2) - 4.0 * at(1) + 6.0 * own - 4.0 * at(-1) + at(-2)
    return first, fourth


def local(
    adjoint_start,
    objective_grad,
    spectral_radius,
    local_step,
    flux_jacobian,
    face_orient,
    wall_count,
    face_patch,
    face_area,
    force_weight,
):
    fields, rows_i, rows_j, depth = adjoint_start.shape
    patch_total = P_DEV * lax.axis_size("bx") * lax.axis_size("by")
    low_flag = face_orient[0, 0]
    high_flag = face_orient[0, 1]
    position = jnp.arange(rows_i)[:, None] * rows_j + jnp.arange(rows_j)[None, :]
    live = (position < wall_count[0, 0]).astype(jnp.float32)
    weighted_area = live * face_area
    wall_adjoint = jnp.einsum(
        "f,fxy->xy", force_weight, adjoint_start[:, :, :, 0], precision=lax.Precision.HIGHEST
    )
    wall_value = (weighted_area * wall_adjoint).reshape(-1)
    patch_ids = face_patch.reshape(-1)
    table = (patch_ids[:, None] == jnp.arange(patch_total)[None, :]).astype(jnp.float32)
    local_sum = jnp.dot(wall_value, table, precision=lax.Precision.HIGHEST)
    local_area = jnp.dot(weighted_area.reshape(-1), table, precision=lax.Precision.HIGHEST)
    summed = butterfly_sum(jnp.concatenate([local_sum, local_area]), ("bx", "by"))

    step_area = local_step[:, :, 0] * weighted_area
    lane = jnp.arange(depth)[None, None, :]
    column = jnp.where(
        lane == 0,
        step_area[:, :, None],
        jnp.where(lane == 1, face_patch.astype(jnp.float32)[:, :, None], 0.0),
    )[None]

    radius = spectral_radius
    with jax.named_scope("first"):
        rims, col_rims = halos(adjoint_start, low_flag, high_flag, column)
        col_lo_i, col_hi_i, col_lo_j, col_hi_j = (
            jnp.stack([rim[0, ..., 0], rim[0, ..., 1]]) for rim in col_rims
        )
        section_part = adjoint_start - 0.5 * local_step * (
            operate(adjoint_start, rims, radius, flux_jacobian) + objective_grad
        )
    with jax.named_scope("second"):
        rims, _ = halos(section_part, low_flag, high_flag)
        next_part = adjoint_start - local_step * (
            operate(section_part, rims, radius, flux_jacobian) + objective_grad
        )
    summed, next_part = lax.optimization_barrier((summed, next_part))

    every_force = summed[:patch_total] / (1.0 + summed[patch_total : 2 * patch_total])
    start_own = lax.axis_index(("bx", "by")) * P_DEV
    patch_force = lax.dynamic_slice_in_dim(every_force, start_own, P_DEV, 0)

    def force_of(ids):
        flat = ids.reshape(-1, 1).astype(jnp.int32)
        hit = (flat == jnp.arange(patch_total)[None, :]).astype(jnp.float32)
        return jnp.dot(hit, every_force, precision=lax.Precision.HIGHEST).reshape(ids.shape)

    ids = jnp.concatenate(
        [face_patch.reshape(-1).astype(jnp.float32)]
        + [rim[1].reshape(-1) for rim in (col_lo_i, col_hi_i, col_lo_j, col_hi_j)]
    )
    forces = force_of(ids)
    cut = rows_i * rows_j
    face_force = weighted_area * forces[:cut].reshape(rows_i, rows_j)
    g_own = local_step[:, :, 0] * face_force
    rim_forces = []
    for rim in (col_lo_i, col_hi_i, col_lo_j, col_hi_j):
        size = rim[1].size
        rim_forces.append(rim[0] * forces[cut : cut + size].reshape(rim[1].shape))
        cut += size
    g_lo_i, g_hi_i, g_lo_j, g_hi_j = rim_forces
    zero_i = jnp.zeros_like(g_lo_i)
    first_i0, fourth_i0 = plane_stencil(
        g_own,
        jnp.where(low_flag == 1, zero_i, g_lo_i),
        jnp.where(high_flag == 1, zero_i, g_hi_i),
        0,
    )
    first_ik, fourth_ik = plane_stencil(
        jnp.zeros_like(g_own),
        jnp.where(low_flag == 1, g_lo_i, zero_i),
        jnp.where(high_flag == 1, g_hi_i, zero_i),
        0,
    )
    first_j, fourth_j = plane_stencil(g_own, g_lo_j, g_hi_j, 1)

    kk = jnp.arange(depth)[None, None, :]
    at0 = kk == 0
    atk = kk == depth - 1
    first_i = jnp.where(at0, first_i0[:, :, None], jnp.where(atk, first_ik[:, :, None], 0.0))
    fourth_i = jnp.where(at0, fourth_i0[:, :, None], jnp.where(atk, fourth_ik[:, :, None], 0.0))
    first_j3 = jnp.where(at0, first_j[:, :, None], 0.0)
    fourth_j3 = jnp.where(at0, fourth_j[:, :, None], 0.0)
    g3 = g_own[:, :, None]
    sum_k = jnp.where(kk == 1, g3, 0.0)
    fourth_k = jnp.where(at0, 6.0 * g3, jnp.where(kk == 1, -4.0 * g3, jnp.where(kk == 2, g3, 0.0)))
    wall3 = jnp.where(at0, face_force[:, :, None], 0.0)

    coupled_w = jnp.einsum(
        "dfg,f->dg", flux_jacobian, force_weight, precision=lax.Precision.HIGHEST
    )[:, :, None, None, None]
    weight = force_weight[:, None, None, None]
    spread = (
        radius[0] * (0.5 * coupled_w[0] * first_i + EPS * weight * fourth_i)
        + radius[1] * (0.5 * coupled_w[1] * first_j3 + EPS * weight * fourth_j3)
        + radius[2] * (0.5 * coupled_w[2] * sum_k + EPS * weight * fourth_k)
    )
    correction = weight * wall3 - 0.5 * spread
    adjoint_next = next_part - local_step * correction
    return (adjoint_next, patch_force)


def solution(mesh):
    in_specs = (
        P(None, "bx", "by", None),
        P(None, "bx", "by", None),
        P(None, "bx", "by", None),
        P("bx", "by", None),
        P(),
        P("bx", None),
        P("bx", "by"),
        P("bx", "by"),
        P("bx", "by"),
        P(),
    )
    out_specs = (P(None, "bx", "by", None), P(("bx", "by")))
    return jax.shard_map(local, mesh=mesh, in_specs=in_specs, out_specs=out_specs, check_vma=False)
```

```python
import jax
import jax.numpy as jnp
from jax import lax
from jax.sharding import PartitionSpec as P

P_DEV = 4

EPS = 0.1


def neighbour_rims(shard, axis, dim, width):
    devices, length = lax.axis_size(axis), shard.shape[dim]
    up = [(i, i + 1) for i in range(devices - 1)]
    down = [(j, i) for i, j in up]
    last = lax.slice_in_dim(shard, length - width, length, axis=dim)
    first = lax.slice_in_dim(shard, 0, width, axis=dim)
    before = lax.ppermute(last, axis, up)
    after = lax.ppermute(first, axis, down)
    return before, after


def butterfly_sum(x, axes):
    for axis in axes:
        devices = lax.axis_size(axis)
        bit = 1
        while bit < devices:
            pairs = [(i, i ^ bit) for i in range(devices)]
            x = x + lax.ppermute(x, axis, pairs)
            bit *= 2
    return x


def halos(field, low_flag, high_flag, extra=None):
    if extra is not None:
        field = jnp.concatenate([field, extra], axis=0)
    lo_i, hi_i = neighbour_rims(field, "bx", 1, 2)
    lo_j, hi_j = neighbour_rims(field, "by", 2, 2)
    extras = None
    if extra is not None:
        count = extra.shape[0]
        extras = tuple(rim[-count:] for rim in (lo_i, hi_i, lo_j, hi_j))
        lo_i, hi_i, lo_j, hi_j = (rim[:-count] for rim in (lo_i, hi_i, lo_j, hi_j))
    lo_i = jnp.where(low_flag == 1, jnp.flip(lo_i, 3), lo_i)
    hi_i = jnp.where(high_flag == 1, jnp.flip(hi_i, 3), hi_i)
    return (lo_i, hi_i, lo_j, hi_j), extras


def operate(center, rims, radius, flux_jacobian):
    lo_i, hi_i, lo_j, hi_j = rims
    rows_i, rows_j, depth = center.shape[1:]
    ext_i = jnp.concatenate([lo_i, center, hi_i], axis=1)
    ext_j = jnp.concatenate([lo_j, center, hi_j], axis=2)
    padded_k = jnp.pad(center, ((0, 0), (0, 0), (0, 0), (2, 2)))

    def along_first(offset):
        return ext_i[:, 2 + offset : 2 + offset + rows_i]

    def along_second(offset):
        return ext_j[:, :, 2 + offset : 2 + offset + rows_j]

    def along_third(offset):
        return padded_k[:, :, :, 2 + offset : 2 + offset + depth]

    summed = None
    for direction, slicer in ((0, along_first), (1, along_second), (2, along_third)):
        front_one = slicer(1)
        back_one = slicer(-1)
        fourth = slicer(2) - 4.0 * front_one + 6.0 * center - 4.0 * back_one + slicer(-2)
        diff = front_one + back_one if direction == 2 else front_one - back_one
        jac = flux_jacobian[direction]
        coupled = sum(jac[f][:, None, None, None] * diff[f][None] for f in range(diff.shape[0]))
        term = radius[direction] * (0.5 * coupled + EPS * fourth)
        summed = term if summed is None else summed + term
    return summed


def plane_stencil(own, lo, hi, axis):
    ext = jnp.concatenate([lo, own, hi], axis=axis)
    n = own.shape[axis]

    def at(offset):
        return lax.slice_in_dim(ext, 2 + offset, 2 + offset + n, axis=axis)

    first = at(1) - at(-1)
    fourth = at(2) - 4.0 * at(1) + 6.0 * own - 4.0 * at(-1) + at(-2)
    return first, fourth


def local(
    adjoint_start,
    objective_grad,
    spectral_radius,
    local_step,
    flux_jacobian,
    face_orient,
    wall_count,
    face_patch,
    face_area,
    force_weight,
):
    fields, rows_i, rows_j, depth = adjoint_start.shape
    patch_total = P_DEV * lax.axis_size("bx") * lax.axis_size("by")
    low_flag = face_orient[0, 0]
    high_flag = face_orient[0, 1]
    position = jnp.arange(rows_i)[:, None] * rows_j + jnp.arange(rows_j)[None, :]
    live = (position < wall_count[0, 0]).astype(jnp.float32)
    weighted_area = live * face_area
    lane_zero = (jnp.arange(depth) == 0).astype(jnp.float32)
    weighted_field = jnp.einsum(
        "f,fxyz->xyz", force_weight, adjoint_start, precision=lax.Precision.HIGHEST
    )
    firsts = jnp.einsum(
        "sxyz,z->sxy",
        jnp.stack([weighted_field, local_step]),
        lane_zero,
        precision=lax.Precision.HIGHEST,
    )
    wall_adjoint, step_zero = firsts[0], firsts[1]
    wall_value = weighted_area * wall_adjoint
    table = (face_patch[:, :, None] == jnp.arange(patch_total)[None, None, :]).astype(jnp.float32)
    local_both = jnp.einsum(
        "sxy,xyp->sp",
        jnp.stack([wall_value, weighted_area]),
        table,
        precision=lax.Precision.HIGHEST,
    )
    local_sum, local_area = local_both[0], local_both[1]
    summed = butterfly_sum(jnp.concatenate([local_sum, local_area]), ("bx", "by"))

    step_area = step_zero * weighted_area
    lane = jnp.arange(depth)[None, None, :]
    column = jnp.where(
        lane == 0,
        step_area[:, :, None],
        jnp.where(lane == 1, face_patch.astype(jnp.float32)[:, :, None], 0.0),
    )[None]

    radius = spectral_radius
    with jax.named_scope("first"):
        rims, col_rims = halos(adjoint_start, low_flag, high_flag, column)
        col_lo_i, col_hi_i, col_lo_j, col_hi_j = (
            jnp.stack([rim[0, ..., 0], rim[0, ..., 1]]) for rim in col_rims
        )
        section_part = adjoint_start - 0.5 * local_step * (
            operate(adjoint_start, rims, radius, flux_jacobian) + objective_grad
        )
    with jax.named_scope("second"):
        rims, _ = halos(section_part, low_flag, high_flag)
        next_part = adjoint_start - local_step * (
            operate(section_part, rims, radius, flux_jacobian) + objective_grad
        )
    summed, next_part = lax.optimization_barrier((summed, next_part))

    every_force = summed[:patch_total] / (1.0 + summed[patch_total : 2 * patch_total])
    start_own = lax.axis_index(("bx", "by")) * P_DEV
    patch_force = lax.dynamic_slice_in_dim(every_force, start_own, P_DEV, 0)

    def force_of(ids):
        flat = ids.reshape(-1, 1).astype(jnp.int32)
        hit = (flat == jnp.arange(patch_total)[None, :]).astype(jnp.float32)
        return jnp.dot(hit, every_force, precision=lax.Precision.HIGHEST).reshape(ids.shape)

    ids = jnp.concatenate(
        [face_patch.reshape(-1).astype(jnp.float32)]
        + [rim[1].reshape(-1) for rim in (col_lo_i, col_hi_i, col_lo_j, col_hi_j)]
    )
    forces = force_of(ids)
    cut = rows_i * rows_j
    face_force = weighted_area * forces[:cut].reshape(rows_i, rows_j)
    g_own = step_zero * face_force
    rim_forces = []
    for rim in (col_lo_i, col_hi_i, col_lo_j, col_hi_j):
        size = rim[1].size
        rim_forces.append(rim[0] * forces[cut : cut + size].reshape(rim[1].shape))
        cut += size
    g_lo_i, g_hi_i, g_lo_j, g_hi_j = rim_forces
    zero_i = jnp.zeros_like(g_lo_i)
    first_i0, fourth_i0 = plane_stencil(
        g_own,
        jnp.where(low_flag == 1, zero_i, g_lo_i),
        jnp.where(high_flag == 1, zero_i, g_hi_i),
        0,
    )
    first_ik, fourth_ik = plane_stencil(
        jnp.zeros_like(g_own),
        jnp.where(low_flag == 1, g_lo_i, zero_i),
        jnp.where(high_flag == 1, g_hi_i, zero_i),
        0,
    )
    first_j, fourth_j = plane_stencil(g_own, g_lo_j, g_hi_j, 1)

    kk = jnp.arange(depth)[None, None, :]
    at0 = kk == 0
    atk = kk == depth - 1
    first_i = jnp.where(at0, first_i0[:, :, None], jnp.where(atk, first_ik[:, :, None], 0.0))
    fourth_i = jnp.where(at0, fourth_i0[:, :, None], jnp.where(atk, fourth_ik[:, :, None], 0.0))
    first_j3 = jnp.where(at0, first_j[:, :, None], 0.0)
    fourth_j3 = jnp.where(at0, fourth_j[:, :, None], 0.0)
    g3 = g_own[:, :, None]
    sum_k = jnp.where(kk == 1, g3, 0.0)
    fourth_k = jnp.where(at0, 6.0 * g3, jnp.where(kk == 1, -4.0 * g3, jnp.where(kk == 2, g3, 0.0)))
    wall3 = jnp.where(at0, face_force[:, :, None], 0.0)

    coupled_w = jnp.einsum(
        "dfg,f->dg", flux_jacobian, force_weight, precision=lax.Precision.HIGHEST
    )[:, :, None, None, None]
    weight = force_weight[:, None, None, None]
    spread = (
        radius[0] * (0.5 * coupled_w[0] * first_i + EPS * weight * fourth_i)
        + radius[1] * (0.5 * coupled_w[1] * first_j3 + EPS * weight * fourth_j3)
        + radius[2] * (0.5 * coupled_w[2] * sum_k + EPS * weight * fourth_k)
    )
    correction = weight * wall3 - 0.5 * spread
    adjoint_next = next_part - local_step * correction
    return (adjoint_next, patch_force)


def solution(mesh):
    in_specs = (
        P(None, "bx", "by", None),
        P(None, "bx", "by", None),
        P(None, "bx", "by", None),
        P("bx", "by", None),
        P(),
        P("bx", None),
        P("bx", "by"),
        P("bx", "by"),
        P("bx", "by"),
        P(),
    )
    out_specs = (P(None, "bx", "by", None), P(("bx", "by")))
    return jax.shard_map(local, mesh=mesh, in_specs=in_specs, out_specs=out_specs, check_vma=False)
```

```python
import jax
import jax.numpy as jnp
from jax import lax
from jax.sharding import PartitionSpec as P

P_DEV = 4

EPS = 0.1


def neighbour_rims(shard, axis, dim, width):
    devices, length = lax.axis_size(axis), shard.shape[dim]
    up = [(i, i + 1) for i in range(devices - 1)]
    down = [(j, i) for i, j in up]
    last = lax.slice_in_dim(shard, length - width, length, axis=dim)
    first = lax.slice_in_dim(shard, 0, width, axis=dim)
    before = lax.ppermute(last, axis, up)
    after = lax.ppermute(first, axis, down)
    return before, after


def butterfly_sum(x, axes):
    for axis in axes:
        devices = lax.axis_size(axis)
        bit = 1
        while bit < devices:
            pairs = [(i, i ^ bit) for i in range(devices)]
            x = x + lax.ppermute(x, axis, pairs)
            bit *= 2
    return x


def halos(field, low_flag, high_flag, extra=None):
    if extra is not None:
        field = jnp.concatenate([field, extra], axis=0)
    lo_i, hi_i = neighbour_rims(field, "bx", 1, 2)
    lo_j, hi_j = neighbour_rims(field, "by", 2, 2)
    extras = None
    if extra is not None:
        count = extra.shape[0]
        extras = tuple(rim[-count:] for rim in (lo_i, hi_i, lo_j, hi_j))
        lo_i, hi_i, lo_j, hi_j = (rim[:-count] for rim in (lo_i, hi_i, lo_j, hi_j))
    lo_i = jnp.where(low_flag == 1, jnp.flip(lo_i, 3), lo_i)
    hi_i = jnp.where(high_flag == 1, jnp.flip(hi_i, 3), hi_i)
    return (lo_i, hi_i, lo_j, hi_j), extras


def operate(center, rims, radius, flux_jacobian):
    lo_i, hi_i, lo_j, hi_j = rims
    rows_i, rows_j, depth = center.shape[1:]
    ext_i = jnp.concatenate([lo_i, center, hi_i], axis=1)
    ext_j = jnp.concatenate([lo_j, center, hi_j], axis=2)
    padded_k = jnp.pad(center, ((0, 0), (0, 0), (0, 0), (2, 2)))

    def along_first(offset):
        return ext_i[:, 2 + offset : 2 + offset + rows_i]

    def along_second(offset):
        return ext_j[:, :, 2 + offset : 2 + offset + rows_j]

    def along_third(offset):
        return padded_k[:, :, :, 2 + offset : 2 + offset + depth]

    summed = None
    for direction, slicer in ((0, along_first), (1, along_second), (2, along_third)):
        front_one = slicer(1)
        back_one = slicer(-1)
        fourth = slicer(2) - 4.0 * front_one + 6.0 * center - 4.0 * back_one + slicer(-2)
        diff = front_one + back_one if direction == 2 else front_one - back_one
        jac = flux_jacobian[direction]
        coupled = sum(jac[f][:, None, None, None] * diff[f][None] for f in range(diff.shape[0]))
        term = radius[direction] * (0.5 * coupled + EPS * fourth)
        summed = term if summed is None else summed + term
    return summed


def plane_stencil(own, lo, hi, axis):
    ext = jnp.concatenate([lo, own, hi], axis=axis)
    n = own.shape[axis]

    def at(offset):
        return lax.slice_in_dim(ext, 2 + offset, 2 + offset + n, axis=axis)

    first = at(1) - at(-1)
    fourth = at(2) - 4.0 * at(1) + 6.0 * own - 4.0 * at(-1) + at(-2)
    return first, fourth


def local(
    adjoint_start,
    objective_grad,
    spectral_radius,
    local_step,
    flux_jacobian,
    face_orient,
    wall_count,
    face_patch,
    face_area,
    force_weight,
):
    fields, rows_i, rows_j, depth = adjoint_start.shape
    patch_total = P_DEV * lax.axis_size("bx") * lax.axis_size("by")
    low_flag = face_orient[0, 0]
    high_flag = face_orient[0, 1]
    position = jnp.arange(rows_i)[:, None] * rows_j + jnp.arange(rows_j)[None, :]
    live = (position < wall_count[0, 0]).astype(jnp.float32)
    weighted_area = live * face_area
    lane_zero = (jnp.arange(depth) == 0).astype(jnp.float32)
    weighted_field = jnp.einsum(
        "f,fxyz->xyz", force_weight, adjoint_start, precision=lax.Precision.HIGHEST
    )
    firsts = jnp.einsum(
        "sxyz,z->sxy",
        jnp.stack([weighted_field, local_step]),
        lane_zero,
        precision=lax.Precision.HIGHEST,
    )
    wall_adjoint, step_zero = firsts[0], firsts[1]
    wall_value = weighted_area * wall_adjoint
    table = (face_patch[:, :, None] == jnp.arange(patch_total)[None, None, :]).astype(jnp.float32)
    local_both = jnp.einsum(
        "sxy,xyp->sp",
        jnp.stack([wall_value, weighted_area]),
        table,
        precision=lax.Precision.HIGHEST,
    )
    local_sum, local_area = local_both[0], local_both[1]
    step_area = step_zero * weighted_area
    lane = jnp.arange(depth)[None, None, :]
    column = jnp.where(
        lane == 0,
        step_area[:, :, None],
        jnp.where(lane == 1, face_patch.astype(jnp.float32)[:, :, None], 0.0),
    )[None]

    radius = spectral_radius
    with jax.named_scope("first"):
        rims, col_rims = halos(adjoint_start, low_flag, high_flag, column)
        col_lo_i, col_hi_i, col_lo_j, col_hi_j = (
            jnp.stack([rim[0, ..., 0], rim[0, ..., 1]]) for rim in col_rims
        )
        section_part = adjoint_start - 0.5 * local_step * (
            operate(adjoint_start, rims, radius, flux_jacobian) + objective_grad
        )
    with jax.named_scope("second"):
        rims, _ = halos(section_part, low_flag, high_flag)
    hold = 0.0 * sum(rim[0, 0, 0, 0] for rim in rims)
    summed = butterfly_sum(jnp.concatenate([local_sum, local_area]) + hold, ("bx", "by"))
    with jax.named_scope("second"):
        next_part = adjoint_start - local_step * (
            operate(section_part, rims, radius, flux_jacobian) + objective_grad
        )
    summed, next_part = lax.optimization_barrier((summed, next_part))

    every_force = summed[:patch_total] / (1.0 + summed[patch_total : 2 * patch_total])
    start_own = lax.axis_index(("bx", "by")) * P_DEV
    patch_force = lax.dynamic_slice_in_dim(every_force, start_own, P_DEV, 0)

    def force_of(ids):
        flat = ids.reshape(-1, 1).astype(jnp.int32)
        hit = (flat == jnp.arange(patch_total)[None, :]).astype(jnp.float32)
        return jnp.dot(hit, every_force, precision=lax.Precision.HIGHEST).reshape(ids.shape)

    ids = jnp.concatenate(
        [face_patch.reshape(-1).astype(jnp.float32)]
        + [rim[1].reshape(-1) for rim in (col_lo_i, col_hi_i, col_lo_j, col_hi_j)]
    )
    forces = force_of(ids)
    cut = rows_i * rows_j
    face_force = weighted_area * forces[:cut].reshape(rows_i, rows_j)
    g_own = step_zero * face_force
    rim_forces = []
    for rim in (col_lo_i, col_hi_i, col_lo_j, col_hi_j):
        size = rim[1].size
        rim_forces.append(rim[0] * forces[cut : cut + size].reshape(rim[1].shape))
        cut += size
    g_lo_i, g_hi_i, g_lo_j, g_hi_j = rim_forces
    zero_i = jnp.zeros_like(g_lo_i)
    first_i0, fourth_i0 = plane_stencil(
        g_own,
        jnp.where(low_flag == 1, zero_i, g_lo_i),
        jnp.where(high_flag == 1, zero_i, g_hi_i),
        0,
    )
    first_ik, fourth_ik = plane_stencil(
        jnp.zeros_like(g_own),
        jnp.where(low_flag == 1, g_lo_i, zero_i),
        jnp.where(high_flag == 1, g_hi_i, zero_i),
        0,
    )
    first_j, fourth_j = plane_stencil(g_own, g_lo_j, g_hi_j, 1)

    kk = jnp.arange(depth)[None, None, :]
    at0 = kk == 0
    atk = kk == depth - 1
    first_i = jnp.where(at0, first_i0[:, :, None], jnp.where(atk, first_ik[:, :, None], 0.0))
    fourth_i = jnp.where(at0, fourth_i0[:, :, None], jnp.where(atk, fourth_ik[:, :, None], 0.0))
    first_j3 = jnp.where(at0, first_j[:, :, None], 0.0)
    fourth_j3 = jnp.where(at0, fourth_j[:, :, None], 0.0)
    g3 = g_own[:, :, None]
    sum_k = jnp.where(kk == 1, g3, 0.0)
    fourth_k = jnp.where(at0, 6.0 * g3, jnp.where(kk == 1, -4.0 * g3, jnp.where(kk == 2, g3, 0.0)))
    wall3 = jnp.where(at0, face_force[:, :, None], 0.0)

    coupled_w = jnp.einsum(
        "dfg,f->dg", flux_jacobian, force_weight, precision=lax.Precision.HIGHEST
    )[:, :, None, None, None]
    weight = force_weight[:, None, None, None]
    spread = (
        radius[0] * (0.5 * coupled_w[0] * first_i + EPS * weight * fourth_i)
        + radius[1] * (0.5 * coupled_w[1] * first_j3 + EPS * weight * fourth_j3)
        + radius[2] * (0.5 * coupled_w[2] * sum_k + EPS * weight * fourth_k)
    )
    correction = weight * wall3 - 0.5 * spread
    adjoint_next = next_part - local_step * correction
    return (adjoint_next, patch_force)


def solution(mesh):
    in_specs = (
        P(None, "bx", "by", None),
        P(None, "bx", "by", None),
        P(None, "bx", "by", None),
        P("bx", "by", None),
        P(),
        P("bx", None),
        P("bx", "by"),
        P("bx", "by"),
        P("bx", "by"),
        P(),
    )
    out_specs = (P(None, "bx", "by", None), P(("bx", "by")))
    return jax.shard_map(local, mesh=mesh, in_specs=in_specs, out_specs=out_specs, check_vma=False)
```

```python
import jax
import jax.numpy as jnp
from jax import lax
from jax.sharding import PartitionSpec as P


P_DEV = 4

EPS = 0.1


def neighbour_rims(shard, axis, dim, width):
    devices, length = lax.axis_size(axis), shard.shape[dim]
    up = [(i, i + 1) for i in range(devices - 1)]
    down = [(j, i) for i, j in up]
    last = lax.slice_in_dim(shard, length - width, length, axis=dim)
    first = lax.slice_in_dim(shard, 0, width, axis=dim)
    before = lax.ppermute(last, axis, up)
    after = lax.ppermute(first, axis, down)
    return before, after


def butterfly_sum(x, axes):
    for axis in axes:
        devices = lax.axis_size(axis)
        bit = 1
        while bit < devices:
            pairs = [(i, i ^ bit) for i in range(devices)]
            x = x + lax.ppermute(x, axis, pairs)
            bit *= 2
    return x


def halos(field, low_flag, high_flag, extra=None):
    if extra is not None:
        field = jnp.concatenate([field, extra], axis=0)
    lo_i, hi_i = neighbour_rims(field, "bx", 1, 2)
    lo_j, hi_j = neighbour_rims(field, "by", 2, 2)
    extras = None
    if extra is not None:
        count = extra.shape[0]
        extras = tuple(rim[-count:] for rim in (lo_i, hi_i, lo_j, hi_j))
        lo_i, hi_i, lo_j, hi_j = (rim[:-count] for rim in (lo_i, hi_i, lo_j, hi_j))
    lo_i = jnp.where(low_flag == 1, jnp.flip(lo_i, 3), lo_i)
    hi_i = jnp.where(high_flag == 1, jnp.flip(hi_i, 3), hi_i)
    return (lo_i, hi_i, lo_j, hi_j), extras


def operate(center, rims, radius, flux_jacobian):
    lo_i, hi_i, lo_j, hi_j = rims
    rows_i, rows_j, depth = center.shape[1:]
    ext_i = jnp.concatenate([lo_i, center, hi_i], axis=1)
    ext_j = jnp.concatenate([lo_j, center, hi_j], axis=2)
    padded_k = jnp.pad(center, ((0, 0), (0, 0), (0, 0), (2, 2)))

    def along_first(offset):
        return ext_i[:, 2 + offset : 2 + offset + rows_i]

    def along_second(offset):
        return ext_j[:, :, 2 + offset : 2 + offset + rows_j]

    def along_third(offset):
        return padded_k[:, :, :, 2 + offset : 2 + offset + depth]

    summed = None
    for direction, slicer in ((0, along_first), (1, along_second), (2, along_third)):
        front_one = slicer(1)
        back_one = slicer(-1)
        fourth = slicer(2) - 4.0 * front_one + 6.0 * center - 4.0 * back_one + slicer(-2)
        diff = front_one + back_one if direction == 2 else front_one - back_one
        jac = flux_jacobian[direction]
        coupled = sum(jac[f][:, None, None, None] * diff[f][None] for f in range(diff.shape[0]))
        term = radius[direction] * (0.5 * coupled + EPS * fourth)
        summed = term if summed is None else summed + term
    return summed


def plane_stencil(own, lo, hi, axis):
    ext = jnp.concatenate([lo, own, hi], axis=axis)
    n = own.shape[axis]

    def at(offset):
        return lax.slice_in_dim(ext, 2 + offset, 2 + offset + n, axis=axis)

    first = at(1) - at(-1)
    fourth = at(2) - 4.0 * at(1) + 6.0 * own - 4.0 * at(-1) + at(-2)
    return first, fourth


def local(
    adjoint_start,
    objective_grad,
    spectral_radius,
    local_step,
    flux_jacobian,
    face_orient,
    wall_count,
    face_patch,
    face_area,
    force_weight,
):
    _, rows_i, rows_j, depth = adjoint_start.shape
    patch_total = P_DEV * lax.axis_size("bx") * lax.axis_size("by")
    low_flag = face_orient[0, 0]
    high_flag = face_orient[0, 1]
    position = jnp.arange(rows_i)[:, None] * rows_j + jnp.arange(rows_j)[None, :]
    live = (position < wall_count[0, 0]).astype(jnp.float32)
    weighted_area = live * face_area
    lane_zero = (jnp.arange(depth) == 0).astype(jnp.float32)
    field_zero = jnp.einsum(
        "fxyz,z->fxy", adjoint_start, lane_zero, precision=lax.Precision.HIGHEST
    )
    step_zero = jnp.einsum("xyz,z->xy", local_step, lane_zero, precision=lax.Precision.HIGHEST)
    wall_adjoint = jnp.einsum(
        "f,fxy->xy", force_weight, field_zero, precision=lax.Precision.HIGHEST
    )
    wall_value = weighted_area * wall_adjoint
    table = (face_patch[:, :, None] == jnp.arange(patch_total)[None, None, :]).astype(jnp.float32)
    local_both = jnp.einsum(
        "sxy,xyp->sp",
        jnp.stack([wall_value, weighted_area]),
        table,
        precision=lax.Precision.HIGHEST,
    )
    local_sum, local_area = local_both[0], local_both[1]
    summed = butterfly_sum(jnp.concatenate([local_sum, local_area]), ("bx", "by"))

    step_area = step_zero * weighted_area
    lane = jnp.arange(depth)[None, None, :]
    column = jnp.where(
        lane == 0,
        step_area[:, :, None],
        jnp.where(lane == 1, face_patch.astype(jnp.float32)[:, :, None], 0.0),
    )[None]

    radius = spectral_radius
    rims, col_rims = halos(adjoint_start, low_flag, high_flag, column)
    col_lo_i, col_hi_i, col_lo_j, col_hi_j = (
        jnp.stack([rim[0, ..., 0], rim[0, ..., 1]]) for rim in col_rims
    )
    section_part = adjoint_start - 0.5 * local_step * (
        operate(adjoint_start, rims, radius, flux_jacobian) + objective_grad
    )
    rims, _ = halos(section_part, low_flag, high_flag)
    next_part = adjoint_start - local_step * (
        operate(section_part, rims, radius, flux_jacobian) + objective_grad
    )
    summed, next_part = lax.optimization_barrier((summed, next_part))

    every_force = summed[:patch_total] / (1.0 + summed[patch_total : 2 * patch_total])
    start_own = lax.axis_index(("bx", "by")) * P_DEV
    patch_force = lax.dynamic_slice_in_dim(every_force, start_own, P_DEV, 0)

    def force_of(ids):
        flat = ids.reshape(-1, 1).astype(jnp.int32)
        hit = (flat == jnp.arange(patch_total)[None, :]).astype(jnp.float32)
        return jnp.dot(hit, every_force, precision=lax.Precision.HIGHEST).reshape(ids.shape)

    ids = jnp.concatenate(
        [face_patch.reshape(-1).astype(jnp.float32)]
        + [rim[1].reshape(-1) for rim in (col_lo_i, col_hi_i, col_lo_j, col_hi_j)]
    )
    forces = force_of(ids)
    cut = rows_i * rows_j
    face_force = weighted_area * forces[:cut].reshape(rows_i, rows_j)
    g_own = step_zero * face_force
    rim_forces = []
    for rim in (col_lo_i, col_hi_i, col_lo_j, col_hi_j):
        size = rim[1].size
        rim_forces.append(rim[0] * forces[cut : cut + size].reshape(rim[1].shape))
        cut += size
    g_lo_i, g_hi_i, g_lo_j, g_hi_j = rim_forces
    zero_i = jnp.zeros_like(g_lo_i)
    first_i0, fourth_i0 = plane_stencil(
        g_own,
        jnp.where(low_flag == 1, zero_i, g_lo_i),
        jnp.where(high_flag == 1, zero_i, g_hi_i),
        0,
    )
    first_ik, fourth_ik = plane_stencil(
        jnp.zeros_like(g_own),
        jnp.where(low_flag == 1, g_lo_i, zero_i),
        jnp.where(high_flag == 1, g_hi_i, zero_i),
        0,
    )
    first_j, fourth_j = plane_stencil(g_own, g_lo_j, g_hi_j, 1)

    kk = jnp.arange(depth)[None, None, :]
    at0 = kk == 0
    atk = kk == depth - 1
    first_i = jnp.where(at0, first_i0[:, :, None], jnp.where(atk, first_ik[:, :, None], 0.0))
    fourth_i = jnp.where(at0, fourth_i0[:, :, None], jnp.where(atk, fourth_ik[:, :, None], 0.0))
    first_j3 = jnp.where(at0, first_j[:, :, None], 0.0)
    fourth_j3 = jnp.where(at0, fourth_j[:, :, None], 0.0)
    g3 = g_own[:, :, None]
    sum_k = jnp.where(kk == 1, g3, 0.0)
    fourth_k = jnp.where(at0, 6.0 * g3, jnp.where(kk == 1, -4.0 * g3, jnp.where(kk == 2, g3, 0.0)))
    wall3 = jnp.where(at0, face_force[:, :, None], 0.0)

    coupled_w = jnp.einsum(
        "dfg,f->dg", flux_jacobian, force_weight, precision=lax.Precision.HIGHEST
    )[:, :, None, None, None]
    weight = force_weight[:, None, None, None]
    spread = (
        radius[0] * (0.5 * coupled_w[0] * first_i + EPS * weight * fourth_i)
        + radius[1] * (0.5 * coupled_w[1] * first_j3 + EPS * weight * fourth_j3)
        + radius[2] * (0.5 * coupled_w[2] * sum_k + EPS * weight * fourth_k)
    )
    correction = weight * wall3 - 0.5 * spread
    adjoint_next = next_part - local_step * correction
    return (adjoint_next, patch_force)


def solution(mesh):
    in_specs = (
        P(None, "bx", "by", None),
        P(None, "bx", "by", None),
        P(None, "bx", "by", None),
        P("bx", "by", None),
        P(),
        P("bx", None),
        P("bx", "by"),
        P("bx", "by"),
        P("bx", "by"),
        P(),
    )
    out_specs = (P(None, "bx", "by", None), P(("bx", "by")))

    return jax.shard_map(local, mesh=mesh, in_specs=in_specs, out_specs=out_specs, check_vma=False)
```
